512 devices in a mesh: dp: 64 (over x, z, y_lo), fsdp: 8 (over y_hi, core).
Axes of the slice: x: 4, y: 8 (y_hi: 4, y_lo: 2; y = y_hi * 2 + y_lo), z: 8, core: 2. Of those that a mesh axis runs over, the one named last changes fastest.
Arguments:
- group_qkv: bfloat16 [64, 1024, 6144], P('dp', 'fsdp'), may hold values from -6 to 6
- cache_pool: bfloat16 [8192, 16, 4096], P('dp', None, 'fsdp'), may hold values from -6 to 6
- page_request: int32 [8192], P('dp'), may hold values from 0 to 64, as said below
- request_host: int32 [64], replicated, may hold values from 0 to 63, each once
- out_weight: bfloat16 [2048, 2048], P(('dp', 'fsdp')), may hold values from -0.5 to 0.5
Outputs:
- projected: bfloat16 [64, 1024, 2048], P('dp', 'fsdp')
The draws below stay inside these ranges and needn't reach their ends.
Inputs may be any that keep to these rules, and one draw needn't show every extreme that they name: `page_request`: within the slots of one dp index, at most 2 pages belong to one request, and some request has exactly 2 pages in the slots of every dp index. A request holds 1 to 15 pages, or 64 to 128 pages. Some slot is empty.
All inputs are finite; a program needn't handle non-finite values.
Results may differ from the reference program's by a relative error of at most 0.0053.
Values may be sent and summed in bfloat16 or wider, within the bound.
No kernel may reach another device: no remote copies, remote signals or barrier semaphores. Data moves between devices by JAX's collectives and lax.ppermute only.
A program may use at most 64 MiB of HBM per device.

```python
import math
import jax
import jax.numpy as jnp
from jax import lax

D = 2048
H = 16
HD = 128
PAGE = 16
MOST = 2
SHORT_PAGES = 15
REQS = 64
SLOTS = 128
GROUP = 1024


def draw_page_request(key, part):
    key_long = jax.random.fold_in(key, 11)
    key_full = jax.random.fold_in(key, 12)
    key_short = jax.random.fold_in(key, 13)
    key_drop = jax.random.fold_in(key, 14)
    key_count = jax.random.fold_in(key, 15)
    key_order = jax.random.fold_in(key, 16)
    key_slots = jax.random.fold_in(key, 17)
    request_ids = jnp.arange(REQS, dtype=jnp.int32)
    is_long = jax.random.randint(key_long, (REQS,), 0, 2)
    full_one = jax.random.randint(key_full, (), 0, REQS)
    short_one = (full_one + 1 + jax.random.randint(key_short, (), 0, REQS - 1)) % REQS
    is_long = jnp.where(request_ids == full_one, 1, jnp.where(request_ids == short_one, 0, is_long))
    dropped = (jax.random.randint(key_drop, (REQS, REQS), 0, 8) == 0).astype(jnp.int32)
    long_counts = MOST - dropped
    long_counts = jnp.where(request_ids[None, :] == full_one, MOST, long_counts)
    short_total = jax.random.randint(key_count, (REQS,), 1, SHORT_PAGES + 1)
    orders = jax.vmap(lambda sub: jax.random.permutation(sub, REQS))(jax.random.split(key_order, REQS))
    source_rank = jnp.argsort(orders, axis=1).astype(jnp.int32)
    short_counts = (jnp.transpose(source_rank) < short_total[None, :]).astype(jnp.int32)
    counts = jnp.where(is_long[None, :] == 1, long_counts, short_counts)
    slot_ids = jnp.arange(REQS * MOST, dtype=jnp.int32)
    slot_owner = slot_ids // MOST
    slot_index = slot_ids % MOST
    layout = jnp.where(slot_index[None, :] < counts[:, slot_owner], slot_owner[None, :], REQS)
    shuffles = jax.vmap(lambda sub: jax.random.permutation(sub, REQS * MOST))(jax.random.split(key_slots, REQS))
    shuffled = jnp.take_along_axis(layout, shuffles, axis=1)
    return shuffled.reshape(REQS * REQS * MOST).astype(jnp.int32)


def draw_group_qkv(key, part):
    key_base = jax.random.fold_in(key, 21)
    base = jnp.clip(1.3 * jax.random.normal(key_base, (REQS, GROUP, H, 3, HD), jnp.float32), -6.0, 6.0)
    return base.reshape(REQS, GROUP, H * 3 * HD).astype(jnp.bfloat16)


def spiked(result, stream_key, source, target, blocks, factor):
    def block_of(axis_at):
        return (jnp.arange(result.shape[axis_at]) // (result.shape[axis_at] // blocks)).reshape((-1,) + (1,) * (result.ndim - 1 - axis_at))

    near = jax.random.permutation(stream_key, blocks)[block_of(target)]
    other_side = (block_of(target) + blocks // 2) % blocks
    return jnp.where((block_of(source) == near) | (block_of(source) == other_side), factor * result, result)


def shard_levels(own_key, dims, pieces, least, high):
    level, own = 1.0, jax.random.fold_in(own_key, 6)
    for position, blocks in pieces:
        steps = jnp.exp(jax.random.uniform(jax.random.fold_in(own, position), (blocks,), jnp.float32, least / len(pieces), high / len(pieces)))
        level = level * jnp.repeat(steps, dims[position] // blocks).reshape([-1 if axis == position else 1 for axis in range(len(dims))])
    return level


def scatter_about(key, dims, width, most, cuts=(), held_as=jnp.bfloat16):
    result = jax.random.normal(key, dims, jnp.float32) * width
    if len(cuts) > 0:
        result = shard_levels(key, dims, cuts, -0.22, 0.18) * result
    return jnp.clip(result, min=-most, max=most).astype(held_as)


def gaussian_with(rng, dims, spread, bound, cuts, heavy, held_as=jnp.bfloat16):
    array = spread * jax.random.normal(rng, dims, jnp.float32)
    if cuts:
        array = array * shard_levels(rng, dims, cuts, -0.22, 0.18)
    return jnp.clip(spiked(array, jax.random.fold_in(rng, 3), *heavy), -bound, bound).astype(held_as)


def setup_inputs(seed: int = 0) -> dict:
    arg_keys = jax.random.split(jax.random.key(seed), 6)
    return {
        "group_qkv": draw_group_qkv(jax.random.fold_in(arg_keys[5], 71), 0),
        "cache_pool": scatter_about(arg_keys[1], (REQS * SLOTS, PAGE, H * 2 * HD), 1.3, 6.0, ((0, 64), (2, 8))),
        "page_request": draw_page_request(jax.random.fold_in(arg_keys[5], 71), 0),
        "request_host": jax.random.permutation(arg_keys[3], REQS).astype(jnp.int32),
        "out_weight": gaussian_with(arg_keys[4], (H * HD, D), (H * HD) ** -0.5, 0.5, ((0, 512),), (0, 1, 512, 6.0)),
    }


def reference(group_qkv, cache_pool, page_request, request_host, out_weight):
    requests = request_host.shape[0]
    request_at = jnp.zeros((requests,), jnp.int32).at[request_host].set(jnp.arange(requests, dtype=jnp.int32))
    capacity = MOST * requests
    score_scale = 1.0 / math.sqrt(HD)

    def one_request(inputs):
        group_rows, hosted = inputs
        order = jnp.argsort((page_request != hosted).astype(jnp.int32), stable=True)[:capacity].astype(jnp.int32)
        live_pages = page_request[order] == hosted
        pages = cache_pool[order].reshape(capacity * PAGE, H, 2, HD)
        live_keys = jnp.repeat(live_pages, PAGE)
        group_len = group_rows.shape[0]
        fresh = group_rows.reshape(group_len, H, 3, HD)
        causal = jnp.arange(group_len)[None, :] <= jnp.arange(group_len)[:, None]
        allowed = jnp.concatenate([jnp.broadcast_to(live_keys[None, :], (group_len, capacity * PAGE)), causal], axis=1)

        def one_head(parts):
            queries, keys_cache, values_cache, keys_new, values_new = parts
            all_keys = jnp.concatenate([keys_cache, keys_new], axis=0)
            all_values = jnp.concatenate([values_cache, values_new], axis=0)
            scores = jnp.dot(queries, all_keys.T, preferred_element_type=jnp.float32) * score_scale
            scores = jnp.where(allowed, scores, -jnp.inf)
            row_max = lax.optimization_barrier(jnp.max(scores, axis=1))
            expo = jnp.exp(scores - row_max[:, None])
            row_total = lax.optimization_barrier(jnp.sum(expo, axis=1))
            weights = expo.astype(jnp.bfloat16)
            mixed = jnp.dot(weights, all_values, preferred_element_type=jnp.float32)
            return (mixed / row_total[:, None]).astype(jnp.bfloat16)
        per_head = lax.map(one_head, (jnp.transpose(fresh[:, :, 0], (1, 0, 2)), jnp.transpose(pages[:, :, 0], (1, 0, 2)), jnp.transpose(pages[:, :, 1], (1, 0, 2)), jnp.transpose(fresh[:, :, 1], (1, 0, 2)), jnp.transpose(fresh[:, :, 2], (1, 0, 2))))
        attention = jnp.transpose(per_head, (1, 0, 2)).reshape(group_len, H * HD)
        return jnp.dot(attention, out_weight, preferred_element_type=jnp.float32).astype(jnp.bfloat16)
    return lax.map(one_request, (group_qkv, request_at))
```

```python
import math

import jax
import jax.numpy as jnp
from jax import lax
from jax.sharding import Mesh, PartitionSpec as P

HD = 128
PAGE = 16
MOST = 2


def per_device(group_qkv, cache_pool, page_request, request_host, out_weight):
    fsdp_count = lax.axis_size("fsdp")
    requests = request_host.shape[0]
    slot_count = page_request.shape[0]
    tokens_here = group_qkv.shape[1]
    features = cache_pool.shape[2]
    heads_here = features // (2 * HD)
    score_scale = 1.0 / math.sqrt(HD)
    request_ids = jnp.arange(requests, dtype=jnp.int32)
    member = (page_request[:, None] == request_ids[None, :]).astype(jnp.int32)
    slot_rank = jnp.sum(member * (jnp.cumsum(member, axis=0) - 1), axis=1)
    target_host = jnp.sum(member * request_host[None, :], axis=1)
    is_live = jnp.sum(member, axis=1)
    target_slot = jnp.where(is_live > 0, target_host * MOST + slot_rank, -1)
    chosen = target_slot[:, None] == jnp.arange(requests * MOST, dtype=jnp.int32)[None, :]
    flat_pool = cache_pool.reshape(slot_count, PAGE * features)
    packed = jnp.einsum(
        "sp,sf->pf", chosen.astype(jnp.bfloat16), flat_pool, preferred_element_type=jnp.float32
    )
    packed = packed.astype(jnp.bfloat16).reshape(requests, MOST, PAGE, features)
    occupied = jnp.sum(chosen.astype(jnp.int32), axis=0).reshape(requests, MOST)
    arrived, present = (
        lax.all_to_all(packed, "dp", split_axis=0, concat_axis=0, tiled=True),
        lax.all_to_all(occupied, "dp", split_axis=0, concat_axis=0, tiled=True),
    )
    cached = arrived.reshape(requests * MOST * PAGE, heads_here, 2, HD)
    key_cache = cached[:, :, 0]
    value_cache = cached[:, :, 1]
    live_tokens = jnp.repeat(present.reshape(requests * MOST), PAGE) > 0
    local_qkv = group_qkv.reshape(tokens_here, fsdp_count, heads_here * 3 * HD)
    gathered_qkv = lax.all_to_all(local_qkv, "fsdp", split_axis=1, concat_axis=0, tiled=True)
    group_len = tokens_here * fsdp_count
    gathered_qkv = gathered_qkv.reshape(group_len, heads_here, 3, HD)
    queries = gathered_qkv[:, :, 0]
    new_keys = gathered_qkv[:, :, 1]
    new_values = gathered_qkv[:, :, 2]
    block_rows = min(512, group_len)
    block_count = group_len // block_rows
    query_blocks = queries.reshape(block_count, block_rows, heads_here, HD)

    def attend(inputs):
        query_block, first_row = inputs
        cache_scores = (
            jnp.einsum("qhd,khd->hqk", query_block, key_cache, preferred_element_type=jnp.float32)
            * score_scale
        )
        cache_scores = jnp.where(live_tokens[None, None, :], cache_scores, -jnp.inf)
        group_scores = (
            jnp.einsum("qhd,khd->hqk", query_block, new_keys, preferred_element_type=jnp.float32)
            * score_scale
        )
        causal = jnp.arange(group_len)[None, :] <= first_row + jnp.arange(block_rows)[:, None]
        group_scores = jnp.where(causal[None, :, :], group_scores, -jnp.inf)
        row_max = jnp.maximum(jnp.max(cache_scores, axis=2), jnp.max(group_scores, axis=2))
        cache_expo = jnp.exp(cache_scores - row_max[:, :, None])
        group_expo = jnp.exp(group_scores - row_max[:, :, None])
        row_total = jnp.sum(cache_expo, axis=2) + jnp.sum(group_expo, axis=2)
        mixture = jnp.einsum(
            "hqk,khd->qhd",
            cache_expo.astype(jnp.bfloat16),
            value_cache,
            preferred_element_type=jnp.float32,
        )
        mixture = mixture + jnp.einsum(
            "hqk,khd->qhd",
            group_expo.astype(jnp.bfloat16),
            new_values,
            preferred_element_type=jnp.float32,
        )
        result = mixture / jnp.transpose(row_total)[:, :, None]
        return result.astype(jnp.bfloat16).reshape(block_rows, heads_here * HD)

    starts = jnp.arange(block_count, dtype=jnp.int32) * block_rows
    attn_heads = lax.map(attend, (query_blocks, starts)).reshape(group_len, heads_here * HD)
    tokens_attn = lax.all_to_all(attn_heads, "fsdp", split_axis=0, concat_axis=1, tiled=True)
    summed = jnp.dot(tokens_attn, out_weight, preferred_element_type=jnp.float32)
    return summed.astype(jnp.bfloat16).reshape(1, tokens_here, out_weight.shape[1])


PHYSICAL_SPLIT = {"dp": (("x", 4), ("z", 8), ("y_lo", 2)), "fsdp": (("y_hi", 4), ("core", 2))}


def gather_rows(mesh):
    split = [part for axis in mesh.axis_names for part in PHYSICAL_SPLIT[axis]]
    names = tuple(name for name, _ in split)
    fine = Mesh(mesh.devices.reshape([size for _, size in split]), names)

    def body(block):
        for name in reversed(names):
            block = lax.all_gather(block, name, axis=0, tiled=True)
        return block

    return jax.shard_map(
        body, mesh=fine, in_specs=P(names, None), out_specs=P(), check_vma=False
    )


def solution(mesh):
    split_sizes = [math.prod(s for _, s in PHYSICAL_SPLIT[a]) for a in mesh.axis_names]
    if tuple(split_sizes) == tuple(mesh.devices.shape):
        gather = gather_rows(mesh)
    else:
        gather = jax.shard_map(
            lambda w: lax.all_gather(w, ("dp", "fsdp"), axis=0, tiled=True),
            mesh=mesh, in_specs=P(("dp", "fsdp"), None), out_specs=P(), check_vma=False,
        )
    attend_all = jax.shard_map(
        per_device,
        mesh=mesh,
        in_specs=(
            P("dp", "fsdp", None),
            P("dp", None, "fsdp"),
            P("dp"),
            P(),
            P(),
        ),
        out_specs=P("dp", "fsdp", None),
        check_vma=False,
    )

    def run(group_qkv, cache_pool, page_request, request_host, out_weight):
        return attend_all(group_qkv, cache_pool, page_request, request_host, gather(out_weight))

    return run
```

```python
import math

import jax
import jax.numpy as jnp
from jax import lax
from jax.sharding import Mesh, PartitionSpec as P

HD = 128
PAGE = 16
MOST = 2


def per_device(group_qkv, cache_pool, page_request, request_host, out_weight):
    fsdp_count = lax.axis_size("fsdp")
    requests = request_host.shape[0]
    slot_count = page_request.shape[0]
    tokens_here = group_qkv.shape[1]
    features = cache_pool.shape[2]
    heads_here = features // (2 * HD)
    score_scale = 1.0 / math.sqrt(HD)
    request_ids = jnp.arange(requests, dtype=jnp.int32)
    member = (page_request[:, None] == request_ids[None, :]).astype(jnp.int32)
    slot_rank = jnp.sum(member * (jnp.cumsum(member, axis=0) - 1), axis=1)
    target_host = jnp.sum(member * request_host[None, :], axis=1)
    is_live = jnp.sum(member, axis=1)
    target_slot = jnp.where(is_live > 0, target_host * MOST + slot_rank, -1)
    chosen = target_slot[:, None] == jnp.arange(requests * MOST, dtype=jnp.int32)[None, :]
    flat_pool = cache_pool.reshape(slot_count, PAGE * features)
    packed = jnp.einsum(
        "sp,sf->pf", chosen.astype(jnp.bfloat16), flat_pool, preferred_element_type=jnp.float32
    )
    occupied = jnp.sum(chosen.astype(jnp.int32), axis=0) > 0
    packed = jnp.where(occupied[:, None], packed, jnp.nan)
    packed = packed.astype(jnp.bfloat16).reshape(requests, MOST, PAGE, features)
    arrived = lax.all_to_all(packed, "dp", split_axis=0, concat_axis=0, tiled=True)
    present = jnp.logical_not(jnp.isnan(arrived[:, :, 0, 0]))
    live_tokens = jnp.repeat(present.reshape(requests * MOST), PAGE)
    cached = arrived.reshape(requests * MOST * PAGE, heads_here, 2, HD)
    key_cache = cached[:, :, 0]
    value_cache = jnp.where(live_tokens[:, None, None], cached[:, :, 1], jnp.zeros((), cached.dtype))
    local_qkv = group_qkv.reshape(tokens_here, fsdp_count, heads_here * 3 * HD)
    gathered_qkv = lax.all_to_all(local_qkv, "fsdp", split_axis=1, concat_axis=0, tiled=True)
    group_len = tokens_here * fsdp_count
    gathered_qkv = gathered_qkv.reshape(group_len, heads_here, 3, HD)
    queries = gathered_qkv[:, :, 0]
    new_keys = gathered_qkv[:, :, 1]
    new_values = gathered_qkv[:, :, 2]
    block_rows = min(512, group_len)
    block_count = group_len // block_rows
    query_blocks = queries.reshape(block_count, block_rows, heads_here, HD)

    def attend(inputs):
        query_block, first_row = inputs
        cache_scores = (
            jnp.einsum("qhd,khd->hqk", query_block, key_cache, preferred_element_type=jnp.float32)
            * score_scale
        )
        cache_scores = jnp.where(live_tokens[None, None, :], cache_scores, -jnp.inf)
        group_scores = (
            jnp.einsum("qhd,khd->hqk", query_block, new_keys, preferred_element_type=jnp.float32)
            * score_scale
        )
        causal = jnp.arange(group_len)[None, :] <= first_row + jnp.arange(block_rows)[:, None]
        group_scores = jnp.where(causal[None, :, :], group_scores, -jnp.inf)
        row_max = jnp.maximum(jnp.max(cache_scores, axis=2), jnp.max(group_scores, axis=2))
        cache_expo = jnp.exp(cache_scores - row_max[:, :, None])
        group_expo = jnp.exp(group_scores - row_max[:, :, None])
        row_total = jnp.sum(cache_expo, axis=2) + jnp.sum(group_expo, axis=2)
        mixture = jnp.einsum(
            "hqk,khd->qhd",
            cache_expo.astype(jnp.bfloat16),
            value_cache,
            preferred_element_type=jnp.float32,
        )
        mixture = mixture + jnp.einsum(
            "hqk,khd->qhd",
            group_expo.astype(jnp.bfloat16),
            new_values,
            preferred_element_type=jnp.float32,
        )
        result = mixture / jnp.transpose(row_total)[:, :, None]
        return result.astype(jnp.bfloat16).reshape(block_rows, heads_here * HD)

    starts = jnp.arange(block_count, dtype=jnp.int32) * block_rows
    attn_heads = lax.map(attend, (query_blocks, starts)).reshape(group_len, heads_here * HD)
    tokens_attn = lax.all_to_all(attn_heads, "fsdp", split_axis=0, concat_axis=1, tiled=True)
    summed = jnp.dot(tokens_attn, out_weight, preferred_element_type=jnp.float32)
    return summed.astype(jnp.bfloat16).reshape(1, tokens_here, out_weight.shape[1])


PHYSICAL_SPLIT = {"dp": (("x", 4), ("z", 8), ("y_lo", 2)), "fsdp": (("y_hi", 4), ("core", 2))}


def gather_rows(mesh):
    split = [part for axis in mesh.axis_names for part in PHYSICAL_SPLIT[axis]]
    names = tuple(name for name, _ in split)
    fine = Mesh(mesh.devices.reshape([size for _, size in split]), names)

    def body(block):
        for name in reversed(names):
            block = lax.all_gather(block, name, axis=0, tiled=True)
        return block

    return jax.shard_map(
        body, mesh=fine, in_specs=P(names, None), out_specs=P(), check_vma=False
    )


def solution(mesh):
    split_sizes = [math.prod(s for _, s in PHYSICAL_SPLIT[a]) for a in mesh.axis_names]
    if tuple(split_sizes) == tuple(mesh.devices.shape):
        gather = gather_rows(mesh)
    else:
        gather = jax.shard_map(
            lambda w: lax.all_gather(w, ("dp", "fsdp"), axis=0, tiled=True),
            mesh=mesh, in_specs=P(("dp", "fsdp"), None), out_specs=P(), check_vma=False,
        )
    attend_all = jax.shard_map(
        per_device,
        mesh=mesh,
        in_specs=(
            P("dp", "fsdp", None),
            P("dp", None, "fsdp"),
            P("dp"),
            P(),
            P(),
        ),
        out_specs=P("dp", "fsdp", None),
        check_vma=False,
    )

    def run(group_qkv, cache_pool, page_request, request_host, out_weight):
        return attend_all(group_qkv, cache_pool, page_request, request_host, gather(out_weight))

    return run
```

```python
import math

import jax
import jax.numpy as jnp
from jax import lax
from jax.sharding import Mesh, PartitionSpec as P

HD = 128
PAGE = 16
MOST = 2

PHYSICAL_SPLIT = {"dp": (("x", 4), ("z", 8), ("y_lo", 2)), "fsdp": (("y_hi", 4), ("core", 2))}
DP = tuple(name for name, _ in PHYSICAL_SPLIT["dp"])
FSDP = tuple(name for name, _ in PHYSICAL_SPLIT["fsdp"])


def per_device(group_qkv, cache_pool, page_request, request_host, out_weight, *, fsdp_count, dp_count):
    requests = request_host.shape[0]
    slot_count = page_request.shape[0]
    tokens_here = group_qkv.shape[1]
    features = cache_pool.shape[2]
    heads_here = features // (2 * HD)
    score_scale = 1.0 / math.sqrt(HD)
    rows_here, width = out_weight.shape

    local_qkv = group_qkv.reshape(tokens_here, fsdp_count, heads_here * 3 * HD)
    rider = rows_here * width // tokens_here
    riding = jnp.broadcast_to(
        out_weight.reshape(tokens_here, 1, rider), (tokens_here, fsdp_count, rider)
    )
    outgoing = jnp.concatenate([local_qkv, riding], axis=2)
    gathered = lax.all_to_all(outgoing, FSDP, split_axis=1, concat_axis=0, tiled=True)
    group_len = tokens_here * fsdp_count
    gathered_qkv = gathered[:, 0, : heads_here * 3 * HD].reshape(group_len, heads_here, 3, HD)
    group_rows = gathered[:, 0, heads_here * 3 * HD :].reshape(fsdp_count * rows_here, width)

    half = group_rows.shape[0] // 2
    core = lax.axis_index("core")
    mine = lax.dynamic_slice_in_dim(group_rows, core * half, half, axis=0)
    for name in reversed(DP):
        mine = lax.all_gather(mine, name, axis=0, tiled=True)
    weight = lax.all_gather(mine, "core", axis=0, tiled=True)

    request_ids = jnp.arange(requests, dtype=jnp.int32)
    member = (page_request[:, None] == request_ids[None, :]).astype(jnp.int32)
    slot_rank = jnp.sum(member * (jnp.cumsum(member, axis=0) - 1), axis=1)
    target_host = jnp.sum(member * request_host[None, :], axis=1)
    is_live = jnp.sum(member, axis=1)
    target_slot = jnp.where(is_live > 0, target_host * MOST + slot_rank, -1)
    chosen = target_slot[:, None] == jnp.arange(requests * MOST, dtype=jnp.int32)[None, :]
    flat_pool = cache_pool.reshape(slot_count, PAGE * features)
    packed = jnp.einsum(
        "sp,sf->pf", chosen.astype(jnp.bfloat16), flat_pool, preferred_element_type=jnp.float32
    )
    occupied = jnp.sum(chosen.astype(jnp.int32), axis=0) > 0
    packed = jnp.where(occupied[:, None], packed, jnp.nan)
    packed = packed.astype(jnp.bfloat16).reshape(requests, MOST, PAGE, features)
    arrived = lax.all_to_all(packed, DP, split_axis=0, concat_axis=0, tiled=True)
    present = jnp.logical_not(jnp.isnan(arrived[:, :, 0, 0]))
    live_tokens = jnp.repeat(present.reshape(requests * MOST), PAGE)
    cached = arrived.reshape(requests * MOST * PAGE, heads_here, 2, HD)
    key_cache = cached[:, :, 0]
    value_cache = jnp.where(live_tokens[:, None, None], cached[:, :, 1], jnp.zeros((), cached.dtype))

    queries = gathered_qkv[:, :, 0]
    new_keys = gathered_qkv[:, :, 1]
    new_values = gathered_qkv[:, :, 2]
    block_rows = min(512, group_len)
    block_count = group_len // block_rows
    query_blocks = queries.reshape(block_count, block_rows, heads_here, HD)

    def attend(inputs):
        query_block, first_row = inputs
        cache_scores = (
            jnp.einsum("qhd,khd->hqk", query_block, key_cache, preferred_element_type=jnp.float32)
            * score_scale
        )
        cache_scores = jnp.where(live_tokens[None, None, :], cache_scores, -jnp.inf)
        group_scores = (
            jnp.einsum("qhd,khd->hqk", query_block, new_keys, preferred_element_type=jnp.float32)
            * score_scale
        )
        causal = jnp.arange(group_len)[None, :] <= first_row + jnp.arange(block_rows)[:, None]
        group_scores = jnp.where(causal[None, :, :], group_scores, -jnp.inf)
        row_max = jnp.maximum(jnp.max(cache_scores, axis=2), jnp.max(group_scores, axis=2))
        cache_expo = jnp.exp(cache_scores - row_max[:, :, None])
        group_expo = jnp.exp(group_scores - row_max[:, :, None])
        row_total = jnp.sum(cache_expo, axis=2) + jnp.sum(group_expo, axis=2)
        mixture = jnp.einsum(
            "hqk,khd->qhd",
            cache_expo.astype(jnp.bfloat16),
            value_cache,
            preferred_element_type=jnp.float32,
        )
        mixture = mixture + jnp.einsum(
            "hqk,khd->qhd",
            group_expo.astype(jnp.bfloat16),
            new_values,
            preferred_element_type=jnp.float32,
        )
        result = mixture / jnp.transpose(row_total)[:, :, None]
        return result.astype(jnp.bfloat16).reshape(block_rows, heads_here * HD)

    starts = jnp.arange(block_count, dtype=jnp.int32) * block_rows
    attn_heads = lax.map(attend, (query_blocks, starts)).reshape(group_len, heads_here * HD)
    tokens_attn = lax.all_to_all(attn_heads, FSDP, split_axis=0, concat_axis=1, tiled=True)
    tokens_attn = tokens_attn.reshape(tokens_here, dp_count, 2, half)
    tokens_attn = jnp.transpose(tokens_attn, (0, 2, 1, 3)).reshape(tokens_here, width)
    summed = jnp.dot(tokens_attn, weight, preferred_element_type=jnp.float32)
    return summed.astype(jnp.bfloat16).reshape(1, tokens_here, width)


def solution(mesh):
    split = [part for axis in mesh.axis_names for part in PHYSICAL_SPLIT[axis]]
    fine = Mesh(mesh.devices.reshape([size for _, size in split]), DP + FSDP)
    return jax.shard_map(
        lambda *args: per_device(
            *args, fsdp_count=mesh.shape["fsdp"], dp_count=mesh.shape["dp"]
        ),
        mesh=fine,
        in_specs=(
            P(DP, FSDP, None),
            P(DP, None, FSDP),
            P(DP),
            P(),
            P(DP + FSDP, None),
        ),
        out_specs=P(DP, FSDP, None),
        check_vma=False,
    )
```

```python
import math

import jax
import jax.numpy as jnp
from jax import lax
from jax.sharding import Mesh, PartitionSpec as P

HD = 128
PAGE = 16
MOST = 2

PHYSICAL_SPLIT = {"dp": (("x", 4), ("z", 8), ("y_lo", 2)), "fsdp": (("y_hi", 4), ("core", 2))}
DP = tuple(name for name, _ in PHYSICAL_SPLIT["dp"])
FSDP = tuple(name for name, _ in PHYSICAL_SPLIT["fsdp"])


def per_device(group_qkv, cache_pool, page_request, request_host, out_weight, *, fsdp_count, dp_count):
    requests = request_host.shape[0]
    slot_count = page_request.shape[0]
    tokens_here = group_qkv.shape[1]
    features = cache_pool.shape[2]
    heads_here = features // (2 * HD)
    score_scale = 1.0 / math.sqrt(HD)
    rows_here, width = out_weight.shape

    local_qkv = group_qkv.reshape(tokens_here, fsdp_count, heads_here * 3 * HD)
    rider = rows_here * width // tokens_here
    riding = jnp.broadcast_to(
        out_weight.reshape(tokens_here, 1, rider), (tokens_here, fsdp_count, rider)
    )
    outgoing = jnp.concatenate([local_qkv, riding], axis=2)
    gathered = lax.all_to_all(outgoing, FSDP, split_axis=1, concat_axis=0, tiled=True)
    group_len = tokens_here * fsdp_count
    gathered_qkv = gathered[:, 0, : heads_here * 3 * HD].reshape(group_len, heads_here, 3, HD)
    group_rows = gathered[:, 0, heads_here * 3 * HD :].reshape(fsdp_count * rows_here, width)

    half = group_rows.shape[0] // 2
    core = lax.axis_index("core")
    mine = lax.dynamic_slice_in_dim(group_rows, core * half, half, axis=0)
    mine = lax.all_gather(mine, DP[-1], axis=0, tiled=True)
    mine = lax.all_gather(mine, DP[:-1], axis=0, tiled=True)
    weight = lax.all_gather(mine, "core", axis=0, tiled=True)

    request_ids = jnp.arange(requests, dtype=jnp.int32)
    member = (page_request[:, None] == request_ids[None, :]).astype(jnp.int32)
    slot_rank = jnp.sum(member * (jnp.cumsum(member, axis=0) - 1), axis=1)
    target_host = jnp.sum(member * request_host[None, :], axis=1)
    is_live = jnp.sum(member, axis=1)
    target_slot = jnp.where(is_live > 0, target_host * MOST + slot_rank, -1)
    chosen = target_slot[:, None] == jnp.arange(requests * MOST, dtype=jnp.int32)[None, :]
    flat_pool = cache_pool.reshape(slot_count, PAGE * features)
    packed = jnp.einsum(
        "sp,sf->pf", chosen.astype(jnp.bfloat16), flat_pool, preferred_element_type=jnp.float32
    )
    occupied = jnp.sum(chosen.astype(jnp.int32), axis=0) > 0
    packed = jnp.where(occupied[:, None], packed, jnp.nan)
    packed = packed.astype(jnp.bfloat16).reshape(requests, MOST, PAGE, features)
    arrived = lax.all_to_all(packed, DP, split_axis=0, concat_axis=0, tiled=True)
    present = jnp.logical_not(jnp.isnan(arrived[:, :, 0, 0]))
    live_tokens = jnp.repeat(present.reshape(requests * MOST), PAGE)
    cached = arrived.reshape(requests * MOST * PAGE, heads_here, 2, HD)
    key_cache = cached[:, :, 0]
    value_cache = jnp.where(live_tokens[:, None, None], cached[:, :, 1], jnp.zeros((), cached.dtype))

    queries = gathered_qkv[:, :, 0]
    new_keys = gathered_qkv[:, :, 1]
    new_values = gathered_qkv[:, :, 2]
    block_rows = min(512, group_len)
    block_count = group_len // block_rows
    query_blocks = queries.reshape(block_count, block_rows, heads_here, HD)

    def attend(inputs):
        query_block, first_row = inputs
        cache_scores = (
            jnp.einsum("qhd,khd->hqk", query_block, key_cache, preferred_element_type=jnp.float32)
            * score_scale
        )
        cache_scores = jnp.where(live_tokens[None, None, :], cache_scores, -jnp.inf)
        group_scores = (
            jnp.einsum("qhd,khd->hqk", query_block, new_keys, preferred_element_type=jnp.float32)
            * score_scale
        )
        causal = jnp.arange(group_len)[None, :] <= first_row + jnp.arange(block_rows)[:, None]
        group_scores = jnp.where(causal[None, :, :], group_scores, -jnp.inf)
        row_max = jnp.maximum(jnp.max(cache_scores, axis=2), jnp.max(group_scores, axis=2))
        cache_expo = jnp.exp(cache_scores - row_max[:, :, None])
        group_expo = jnp.exp(group_scores - row_max[:, :, None])
        row_total = jnp.sum(cache_expo, axis=2) + jnp.sum(group_expo, axis=2)
        mixture = jnp.einsum(
            "hqk,khd->qhd",
            cache_expo.astype(jnp.bfloat16),
            value_cache,
            preferred_element_type=jnp.float32,
        )
        mixture = mixture + jnp.einsum(
            "hqk,khd->qhd",
            group_expo.astype(jnp.bfloat16),
            new_values,
            preferred_element_type=jnp.float32,
        )
        result = mixture / jnp.transpose(row_total)[:, :, None]
        return result.astype(jnp.bfloat16).reshape(block_rows, heads_here * HD)

    starts = jnp.arange(block_count, dtype=jnp.int32) * block_rows
    attn_heads = lax.map(attend, (query_blocks, starts)).reshape(group_len, heads_here * HD)
    tokens_attn = lax.all_to_all(attn_heads, FSDP, split_axis=0, concat_axis=1, tiled=True)
    tokens_attn = tokens_attn.reshape(tokens_here, dp_count, 2, half)
    tokens_attn = jnp.transpose(tokens_attn, (0, 2, 1, 3)).reshape(tokens_here, width)
    summed = jnp.dot(tokens_attn, weight, preferred_element_type=jnp.float32)
    return summed.astype(jnp.bfloat16).reshape(1, tokens_here, width)


def solution(mesh):
    split = [part for axis in mesh.axis_names for part in PHYSICAL_SPLIT[axis]]
    fine = Mesh(mesh.devices.reshape([size for _, size in split]), DP + FSDP)
    return jax.shard_map(
        lambda *args: per_device(
            *args, fsdp_count=mesh.shape["fsdp"], dp_count=mesh.shape["dp"]
        ),
        mesh=fine,
        in_specs=(
            P(DP, FSDP, None),
            P(DP, None, FSDP),
            P(DP),
            P(),
            P(DP + FSDP, None),
        ),
        out_specs=P(DP, FSDP, None),
        check_vma=False,
    )
```

```python
import math

import jax
import jax.numpy as jnp
from jax import lax
from jax.sharding import Mesh, PartitionSpec as P

HD = 128
PAGE = 16
MOST = 2

PHYSICAL_SPLIT = {"dp": (("x", 4), ("z", 8), ("y_lo", 2)), "fsdp": (("y_hi", 4), ("core", 2))}
DP = tuple(name for name, _ in PHYSICAL_SPLIT["dp"])
FSDP = tuple(name for name, _ in PHYSICAL_SPLIT["fsdp"])


def per_device(group_qkv, cache_pool, page_request, request_host, out_weight, *, fsdp_count, dp_count):
    requests = request_host.shape[0]
    slot_count = page_request.shape[0]
    tokens_here = group_qkv.shape[1]
    features = cache_pool.shape[2]
    heads_here = features // (2 * HD)
    score_scale = 1.0 / math.sqrt(HD)
    width = out_weight.shape[1]

    weight = out_weight
    for name in reversed(DP[2:] + FSDP):
        weight = lax.all_gather(weight, name, axis=0, tiled=True)
    weight, group_qkv = lax.optimization_barrier((weight, group_qkv))
    weight = lax.all_gather(weight, DP[1], axis=0, tiled=True)

    local_qkv = group_qkv.reshape(tokens_here, fsdp_count, heads_here * 3 * HD)
    gathered_qkv = lax.all_to_all(local_qkv, FSDP, split_axis=1, concat_axis=0, tiled=True)
    group_len = tokens_here * fsdp_count
    gathered_qkv = gathered_qkv.reshape(group_len, heads_here, 3, HD)

    request_ids = jnp.arange(requests, dtype=jnp.int32)
    member = (page_request[:, None] == request_ids[None, :]).astype(jnp.int32)
    slot_rank = jnp.sum(member * (jnp.cumsum(member, axis=0) - 1), axis=1)
    target_host = jnp.sum(member * request_host[None, :], axis=1)
    is_live = jnp.sum(member, axis=1)
    target_slot = jnp.where(is_live > 0, target_host * MOST + slot_rank, -1)
    chosen = target_slot[:, None] == jnp.arange(requests * MOST, dtype=jnp.int32)[None, :]
    flat_pool = cache_pool.reshape(slot_count, PAGE * features)
    packed = jnp.einsum(
        "sp,sf->pf", chosen.astype(jnp.bfloat16), flat_pool, preferred_element_type=jnp.float32
    )
    occupied = jnp.sum(chosen.astype(jnp.int32), axis=0) > 0
    packed = jnp.where(occupied[:, None], packed, jnp.nan)
    packed = packed.astype(jnp.bfloat16).reshape(requests, MOST, PAGE, features)
    weight, packed = lax.optimization_barrier((weight, packed))
    weight = lax.all_gather(weight, DP[0], axis=0, tiled=True)
    arrived = lax.all_to_all(packed, DP, split_axis=0, concat_axis=0, tiled=True)
    present = jnp.logical_not(jnp.isnan(arrived[:, :, 0, 0]))
    live_tokens = jnp.repeat(present.reshape(requests * MOST), PAGE)
    cached = arrived.reshape(requests * MOST * PAGE, heads_here, 2, HD)
    key_cache = cached[:, :, 0]
    value_cache = jnp.where(live_tokens[:, None, None], cached[:, :, 1], jnp.zeros((), cached.dtype))

    queries = gathered_qkv[:, :, 0]
    new_keys = gathered_qkv[:, :, 1]
    new_values = gathered_qkv[:, :, 2]
    block_rows = min(512, group_len)
    block_count = group_len // block_rows
    query_blocks = queries.reshape(block_count, block_rows, heads_here, HD)

    def attend(inputs):
        query_block, first_row = inputs
        cache_scores = (
            jnp.einsum("qhd,khd->hqk", query_block, key_cache, preferred_element_type=jnp.float32)
            * score_scale
        )
        cache_scores = jnp.where(live_tokens[None, None, :], cache_scores, -jnp.inf)
        group_scores = (
            jnp.einsum("qhd,khd->hqk", query_block, new_keys, preferred_element_type=jnp.float32)
            * score_scale
        )
        causal = jnp.arange(group_len)[None, :] <= first_row + jnp.arange(block_rows)[:, None]
        group_scores = jnp.where(causal[None, :, :], group_scores, -jnp.inf)
        row_max = jnp.maximum(jnp.max(cache_scores, axis=2), jnp.max(group_scores, axis=2))
        cache_expo = jnp.exp(cache_scores - row_max[:, :, None])
        group_expo = jnp.exp(group_scores - row_max[:, :, None])
        row_total = jnp.sum(cache_expo, axis=2) + jnp.sum(group_expo, axis=2)
        mixture = jnp.einsum(
            "hqk,khd->qhd",
            cache_expo.astype(jnp.bfloat16),
            value_cache,
            preferred_element_type=jnp.float32,
        )
        mixture = mixture + jnp.einsum(
            "hqk,khd->qhd",
            group_expo.astype(jnp.bfloat16),
            new_values,
            preferred_element_type=jnp.float32,
        )
        result = mixture / jnp.transpose(row_total)[:, :, None]
        return result.astype(jnp.bfloat16).reshape(block_rows, heads_here * HD)

    starts = jnp.arange(block_count, dtype=jnp.int32) * block_rows
    attn_heads = lax.map(attend, (query_blocks, starts)).reshape(group_len, heads_here * HD)
    tokens_attn = lax.all_to_all(attn_heads, FSDP, split_axis=0, concat_axis=1, tiled=True)
    summed = jnp.dot(tokens_attn, weight, preferred_element_type=jnp.float32)
    return summed.astype(jnp.bfloat16).reshape(1, tokens_here, width)


def solution(mesh):
    split = [part for axis in mesh.axis_names for part in PHYSICAL_SPLIT[axis]]
    fine = Mesh(mesh.devices.reshape([size for _, size in split]), DP + FSDP)
    return jax.shard_map(
        lambda *args: per_device(
            *args, fsdp_count=mesh.shape["fsdp"], dp_count=mesh.shape["dp"]
        ),
        mesh=fine,
        in_specs=(
            P(DP, FSDP, None),
            P(DP, None, FSDP),
            P(DP),
            P(),
            P(DP + FSDP, None),
        ),
        out_specs=P(DP, FSDP, None),
        check_vma=False,
    )
```

```python
import functools
import math

import jax
import jax.numpy as jnp
from jax import lax
from jax.experimental import pallas as pl
from jax.experimental.pallas import tpu as pltpu
from jax.sharding import Mesh, PartitionSpec as P

HD = 128
PAGE = 16
MOST = 2

PHYSICAL_SPLIT = {"dp": (("x", 4), ("z", 8), ("y_lo", 2)), "fsdp": (("y_hi", 4), ("core", 2))}
DP = tuple(name for name, _ in PHYSICAL_SPLIT["dp"])
FSDP = tuple(name for name, _ in PHYSICAL_SPLIT["fsdp"])


def attention_kernel(q_ref, kc_ref, vc_ref, kn_ref, vn_ref, live_row_ref, live_col_ref, out_ref, *, scale):
    rows = q_ref.shape[0]
    first = pl.program_id(1) * rows
    contract = (((1,), (1,)), ((), ()))
    q = q_ref[...]
    cache_scores = lax.dot_general(q, kc_ref[...], contract, preferred_element_type=jnp.float32) * scale
    cache_scores = jnp.where(live_row_ref[...] > 0, cache_scores, -jnp.inf)
    group_scores = lax.dot_general(q, kn_ref[...], contract, preferred_element_type=jnp.float32) * scale
    row = first + lax.broadcasted_iota(jnp.int32, group_scores.shape, 0)
    col = lax.broadcasted_iota(jnp.int32, group_scores.shape, 1)
    group_scores = jnp.where(col <= row, group_scores, -jnp.inf)
    row_max = jnp.maximum(
        jnp.max(cache_scores, axis=1, keepdims=True), jnp.max(group_scores, axis=1, keepdims=True)
    )
    cache_expo = jnp.exp(cache_scores - row_max)
    group_expo = jnp.exp(group_scores - row_max)
    row_total = jnp.sum(cache_expo, axis=1, keepdims=True) + jnp.sum(group_expo, axis=1, keepdims=True)
    values = jnp.where(live_col_ref[...] > 0, vc_ref[...], jnp.zeros((), vc_ref.dtype))
    mixture = jnp.dot(cache_expo.astype(jnp.bfloat16), values, preferred_element_type=jnp.float32)
    mixture = mixture + jnp.dot(
        group_expo.astype(jnp.bfloat16), vn_ref[...], preferred_element_type=jnp.float32
    )
    out_ref[...] = (mixture / row_total).astype(out_ref.dtype)


def attention(qkv, cache, live, heads, block_rows):
    group = qkv.shape[0]
    keys = cache.shape[0]
    live = live.astype(jnp.float32)
    flops = 4 * heads * group * (keys + group) * HD
    return pl.pallas_call(
        functools.partial(attention_kernel, scale=1.0 / math.sqrt(HD)),
        grid=(heads, group // block_rows),
        in_specs=[
            pl.BlockSpec((block_rows, HD), lambda h, b: (b, 3 * h)),
            pl.BlockSpec((keys, HD), lambda h, b: (0, 2 * h)),
            pl.BlockSpec((keys, HD), lambda h, b: (0, 2 * h + 1)),
            pl.BlockSpec((group, HD), lambda h, b: (0, 3 * h + 1)),
            pl.BlockSpec((group, HD), lambda h, b: (0, 3 * h + 2)),
            pl.BlockSpec((1, keys), lambda h, b: (0, 0)),
            pl.BlockSpec((keys, 1), lambda h, b: (0, 0)),
        ],
        out_specs=pl.BlockSpec((block_rows, HD), lambda h, b: (b, h)),
        out_shape=jax.ShapeDtypeStruct((group, heads * HD), qkv.dtype),
        cost_estimate=pl.CostEstimate(
            flops=flops,
            transcendentals=heads * group * (keys + group),
            bytes_accessed=2 * (qkv.size + cache.size + group * heads * HD),
        ),
    )(qkv, cache, cache, qkv, qkv, live.reshape(1, keys), live.reshape(keys, 1))


def per_device(group_qkv, cache_pool, page_request, request_host, out_weight, *, fsdp_count, dp_count):
    requests = request_host.shape[0]
    slot_count = page_request.shape[0]
    tokens_here = group_qkv.shape[1]
    features = cache_pool.shape[2]
    heads_here = features // (2 * HD)
    score_scale = 1.0 / math.sqrt(HD)
    width = out_weight.shape[1]

    weight = out_weight
    for name in reversed(DP[2:] + FSDP):
        weight = lax.all_gather(weight, name, axis=0, tiled=True)
    weight, group_qkv = lax.optimization_barrier((weight, group_qkv))
    weight = lax.all_gather(weight, DP[1], axis=0, tiled=True)

    local_qkv = group_qkv.reshape(tokens_here, fsdp_count, heads_here * 3 * HD)
    gathered_qkv = lax.all_to_all(local_qkv, FSDP, split_axis=1, concat_axis=0, tiled=True)
    group_len = tokens_here * fsdp_count
    gathered_qkv = gathered_qkv.reshape(group_len, heads_here * 3 * HD)

    request_ids = jnp.arange(requests, dtype=jnp.int32)
    member = (page_request[:, None] == request_ids[None, :]).astype(jnp.int32)
    slot_rank = jnp.sum(member * (jnp.cumsum(member, axis=0) - 1), axis=1)
    target_host = jnp.sum(member * request_host[None, :], axis=1)
    is_live = jnp.sum(member, axis=1)
    target_slot = jnp.where(is_live > 0, target_host * MOST + slot_rank, -1)
    chosen = target_slot[:, None] == jnp.arange(requests * MOST, dtype=jnp.int32)[None, :]
    flat_pool = cache_pool.reshape(slot_count, PAGE * features)
    packed = jnp.einsum(
        "sp,sf->pf", chosen.astype(jnp.bfloat16), flat_pool, preferred_element_type=jnp.float32
    )
    occupied = jnp.sum(chosen.astype(jnp.int32), axis=0) > 0
    packed = jnp.where(occupied[:, None], packed, jnp.nan)
    packed = packed.astype(jnp.bfloat16).reshape(requests, MOST, PAGE, features)
    weight, packed, gathered_qkv = lax.optimization_barrier((weight, packed, gathered_qkv))
    weight = lax.all_gather(weight, DP[0], axis=0, tiled=True)
    arrived = lax.all_to_all(packed, DP, split_axis=0, concat_axis=0, tiled=True)
    present = jnp.logical_not(jnp.isnan(arrived[:, :, 0, 0]))
    live_tokens = jnp.repeat(present.reshape(requests * MOST), PAGE)
    cached = arrived.reshape(requests * MOST * PAGE, features)
    attn_heads = attention(gathered_qkv, cached, live_tokens, heads_here, min(256, group_len))
    tokens_attn = lax.all_to_all(attn_heads, FSDP, split_axis=0, concat_axis=1, tiled=True)
    summed = jnp.dot(tokens_attn, weight, preferred_element_type=jnp.float32)
    return summed.astype(jnp.bfloat16).reshape(1, tokens_here, width)


def solution(mesh):
    split = [part for axis in mesh.axis_names for part in PHYSICAL_SPLIT[axis]]
    fine = Mesh(mesh.devices.reshape([size for _, size in split]), DP + FSDP)
    return jax.shard_map(
        lambda *args: per_device(
            *args, fsdp_count=mesh.shape["fsdp"], dp_count=mesh.shape["dp"]
        ),
        mesh=fine,
        in_specs=(
            P(DP, FSDP, None),
            P(DP, None, FSDP),
            P(DP),
            P(),
            P(DP + FSDP, None),
        ),
        out_specs=P(DP, FSDP, None),
        check_vma=False,
    )
```

```python
import functools
import math

import jax
import jax.numpy as jnp
from jax import lax
from jax.experimental import pallas as pl
from jax.experimental.pallas import tpu as pltpu
from jax.sharding import Mesh, PartitionSpec as P

HD = 128
PAGE = 16
MOST = 2

PHYSICAL_SPLIT = {"dp": (("x", 4), ("z", 8), ("y_lo", 2)), "fsdp": (("y_hi", 4), ("core", 2))}
DP = tuple(name for name, _ in PHYSICAL_SPLIT["dp"])
FSDP = tuple(name for name, _ in PHYSICAL_SPLIT["fsdp"])


def attention_kernel(q_ref, kc_ref, vc_ref, kn_ref, vn_ref, live_row_ref, live_col_ref, out_ref, *, scale):
    rows = q_ref.shape[0]
    first = pl.program_id(1) * rows
    contract = (((1,), (1,)), ((), ()))
    q = q_ref[...]
    cache_scores = lax.dot_general(q, kc_ref[...], contract, preferred_element_type=jnp.float32) * scale
    cache_scores = jnp.where(live_row_ref[...] > 0, cache_scores, -jnp.inf)
    group_scores = lax.dot_general(q, kn_ref[...], contract, preferred_element_type=jnp.float32) * scale
    row = first + lax.broadcasted_iota(jnp.int32, group_scores.shape, 0)
    col = lax.broadcasted_iota(jnp.int32, group_scores.shape, 1)
    group_scores = jnp.where(col <= row, group_scores, -jnp.inf)
    row_max = jnp.maximum(
        jnp.max(cache_scores, axis=1, keepdims=True), jnp.max(group_scores, axis=1, keepdims=True)
    )
    cache_expo = jnp.exp(cache_scores - row_max)
    group_expo = jnp.exp(group_scores - row_max)
    row_total = jnp.sum(cache_expo, axis=1, keepdims=True) + jnp.sum(group_expo, axis=1, keepdims=True)
    values = jnp.where(live_col_ref[...] > 0, vc_ref[...], jnp.zeros((), vc_ref.dtype))
    mixture = jnp.dot(cache_expo.astype(jnp.bfloat16), values, preferred_element_type=jnp.float32)
    mixture = mixture + jnp.dot(
        group_expo.astype(jnp.bfloat16), vn_ref[...], preferred_element_type=jnp.float32
    )
    out_ref[...] = (mixture / row_total).astype(out_ref.dtype)


def attention(qkv, cache, live, heads, block_rows):
    group = qkv.shape[0]
    keys = cache.shape[0]
    live = live.astype(jnp.float32)
    flops = 4 * heads * group * (keys + group) * HD
    return pl.pallas_call(
        functools.partial(attention_kernel, scale=1.0 / math.sqrt(HD)),
        grid=(heads, group // block_rows),
        in_specs=[
            pl.BlockSpec((block_rows, HD), lambda h, b: (b, 3 * h)),
            pl.BlockSpec((keys, HD), lambda h, b: (0, 2 * h)),
            pl.BlockSpec((keys, HD), lambda h, b: (0, 2 * h + 1)),
            pl.BlockSpec((group, HD), lambda h, b: (0, 3 * h + 1)),
            pl.BlockSpec((group, HD), lambda h, b: (0, 3 * h + 2)),
            pl.BlockSpec((1, keys), lambda h, b: (0, 0)),
            pl.BlockSpec((keys, 1), lambda h, b: (0, 0)),
        ],
        out_specs=pl.BlockSpec((block_rows, HD), lambda h, b: (b, h)),
        out_shape=jax.ShapeDtypeStruct((group, heads * HD), qkv.dtype),
        cost_estimate=pl.CostEstimate(
            flops=flops,
            transcendentals=heads * group * (keys + group),
            bytes_accessed=2 * (qkv.size + cache.size + group * heads * HD),
        ),
    )(qkv, cache, cache, qkv, qkv, live.reshape(1, keys), live.reshape(keys, 1))


def per_device(group_qkv, cache_pool, page_request, request_host, out_weight, *, fsdp_count, dp_count):
    requests = request_host.shape[0]
    slot_count = page_request.shape[0]
    tokens_here = group_qkv.shape[1]
    features = cache_pool.shape[2]
    heads_here = features // (2 * HD)
    score_scale = 1.0 / math.sqrt(HD)
    width = out_weight.shape[1]

    weight = out_weight
    for name in reversed(DP[2:] + FSDP[:-1]):
        weight = lax.all_gather(weight, name, axis=0, tiled=True)
    weight, group_qkv = lax.optimization_barrier((weight, group_qkv))
    weight = lax.all_gather(weight, DP[1], axis=0, tiled=True)

    local_qkv = group_qkv.reshape(tokens_here, fsdp_count, heads_here * 3 * HD)
    gathered_qkv = lax.all_to_all(local_qkv, FSDP, split_axis=1, concat_axis=0, tiled=True)
    group_len = tokens_here * fsdp_count
    gathered_qkv = gathered_qkv.reshape(group_len, heads_here * 3 * HD)

    request_ids = jnp.arange(requests, dtype=jnp.int32)
    member = (page_request[:, None] == request_ids[None, :]).astype(jnp.int32)
    slot_rank = jnp.sum(member * (jnp.cumsum(member, axis=0) - 1), axis=1)
    target_host = jnp.sum(member * request_host[None, :], axis=1)
    is_live = jnp.sum(member, axis=1)
    target_slot = jnp.where(is_live > 0, target_host * MOST + slot_rank, -1)
    chosen = target_slot[:, None] == jnp.arange(requests * MOST, dtype=jnp.int32)[None, :]
    flat_pool = cache_pool.reshape(slot_count, PAGE * features)
    packed = jnp.einsum(
        "sp,sf->pf", chosen.astype(jnp.bfloat16), flat_pool, preferred_element_type=jnp.float32
    )
    occupied = jnp.sum(chosen.astype(jnp.int32), axis=0) > 0
    packed = jnp.where(occupied[:, None], packed, jnp.nan)
    packed = packed.astype(jnp.bfloat16).reshape(requests, MOST, PAGE, features)
    weight, packed, gathered_qkv = lax.optimization_barrier((weight, packed, gathered_qkv))
    weight = lax.all_gather(weight, DP[0], axis=0, tiled=True)
    arrived = lax.all_to_all(packed, DP, split_axis=0, concat_axis=0, tiled=True)
    weight, arrived = lax.optimization_barrier((weight, arrived))
    weight = lax.all_gather(weight, FSDP[-1], axis=0, tiled=True)
    present = jnp.logical_not(jnp.isnan(arrived[:, :, 0, 0]))
    live_tokens = jnp.repeat(present.reshape(requests * MOST), PAGE)
    cached = arrived.reshape(requests * MOST * PAGE, features)
    attn_heads = attention(gathered_qkv, cached, live_tokens, heads_here, min(256, group_len))
    tokens_attn = lax.all_to_all(attn_heads, FSDP, split_axis=0, concat_axis=1, tiled=True)
    cores = lax.axis_size(FSDP[-1])
    rows_here = out_weight.shape[0]
    tokens_attn = tokens_attn.reshape(tokens_here, width // (cores * rows_here), cores, rows_here)
    tokens_attn = jnp.transpose(tokens_attn, (0, 2, 1, 3)).reshape(tokens_here, width)
    summed = jnp.dot(tokens_attn, weight, preferred_element_type=jnp.float32)
    return summed.astype(jnp.bfloat16).reshape(1, tokens_here, width)


def solution(mesh):
    split = [part for axis in mesh.axis_names for part in PHYSICAL_SPLIT[axis]]
    fine = Mesh(mesh.devices.reshape([size for _, size in split]), DP + FSDP)
    return jax.shard_map(
        lambda *args: per_device(
            *args, fsdp_count=mesh.shape["fsdp"], dp_count=mesh.shape["dp"]
        ),
        mesh=fine,
        in_specs=(
            P(DP, FSDP, None),
            P(DP, None, FSDP),
            P(DP),
            P(),
            P(DP + FSDP, None),
        ),
        out_specs=P(DP, FSDP, None),
        check_vma=False,
    )
```

```python
import functools
import math

import jax
import jax.numpy as jnp
from jax import lax
from jax.experimental import pallas as pl
from jax.experimental.pallas import tpu as pltpu
from jax.sharding import Mesh, PartitionSpec as P

HD = 128
PAGE = 16
MOST = 2

PHYSICAL_SPLIT = {"dp": (("x", 4), ("z", 8), ("y_lo", 2)), "fsdp": (("y_hi", 4), ("core", 2))}
DP = tuple(name for name, _ in PHYSICAL_SPLIT["dp"])
FSDP = tuple(name for name, _ in PHYSICAL_SPLIT["fsdp"])


def attention_kernel(q_ref, kc_ref, vc_ref, kn_ref, vn_ref, live_row_ref, live_col_ref, out_ref, *, scale):
    rows = q_ref.shape[0]
    first = pl.program_id(1) * rows
    contract = (((1,), (1,)), ((), ()))
    q = q_ref[...]
    cache_scores = lax.dot_general(q, kc_ref[...], contract, preferred_element_type=jnp.float32) * scale
    cache_scores = jnp.where(live_row_ref[...] > 0, cache_scores, -jnp.inf)
    group_scores = lax.dot_general(q, kn_ref[...], contract, preferred_element_type=jnp.float32) * scale
    row = first + lax.broadcasted_iota(jnp.int32, group_scores.shape, 0)
    col = lax.broadcasted_iota(jnp.int32, group_scores.shape, 1)
    group_scores = jnp.where(col <= row, group_scores, -jnp.inf)
    row_max = jnp.maximum(
        jnp.max(cache_scores, axis=1, keepdims=True), jnp.max(group_scores, axis=1, keepdims=True)
    )
    cache_expo = jnp.exp(cache_scores - row_max)
    group_expo = jnp.exp(group_scores - row_max)
    row_total = jnp.sum(cache_expo, axis=1, keepdims=True) + jnp.sum(group_expo, axis=1, keepdims=True)
    values = jnp.where(live_col_ref[...] > 0, vc_ref[...], jnp.zeros((), vc_ref.dtype))
    mixture = jnp.dot(cache_expo.astype(jnp.bfloat16), values, preferred_element_type=jnp.float32)
    mixture = mixture + jnp.dot(
        group_expo.astype(jnp.bfloat16), vn_ref[...], preferred_element_type=jnp.float32
    )
    out_ref[...] = (mixture / row_total).astype(out_ref.dtype)


def attention(qkv, cache, live, heads, block_rows):
    group = qkv.shape[0]
    keys = cache.shape[0]
    live = live.astype(jnp.float32)
    flops = 4 * heads * group * (keys + group) * HD
    return pl.pallas_call(
        functools.partial(attention_kernel, scale=1.0 / math.sqrt(HD)),
        grid=(heads, group // block_rows),
        in_specs=[
            pl.BlockSpec((block_rows, HD), lambda h, b: (b, 3 * h)),
            pl.BlockSpec((keys, HD), lambda h, b: (0, 2 * h)),
            pl.BlockSpec((keys, HD), lambda h, b: (0, 2 * h + 1)),
            pl.BlockSpec((group, HD), lambda h, b: (0, 3 * h + 1)),
            pl.BlockSpec((group, HD), lambda h, b: (0, 3 * h + 2)),
            pl.BlockSpec((1, keys), lambda h, b: (0, 0)),
            pl.BlockSpec((keys, 1), lambda h, b: (0, 0)),
        ],
        out_specs=pl.BlockSpec((block_rows, HD), lambda h, b: (b, h)),
        out_shape=jax.ShapeDtypeStruct((group, heads * HD), qkv.dtype),
        cost_estimate=pl.CostEstimate(
            flops=flops,
            transcendentals=heads * group * (keys + group),
            bytes_accessed=2 * (qkv.size + cache.size + group * heads * HD),
        ),
    )(qkv, cache, cache, qkv, qkv, live.reshape(1, keys), live.reshape(keys, 1))


def per_device(group_qkv, cache_pool, page_request, request_host, out_weight, *, fsdp_count, dp_count):
    requests = request_host.shape[0]
    slot_count = page_request.shape[0]
    tokens_here = group_qkv.shape[1]
    features = cache_pool.shape[2]
    heads_here = features // (2 * HD)
    score_scale = 1.0 / math.sqrt(HD)
    width = out_weight.shape[1]

    weight = out_weight
    for name in (FSDP[1], DP[2]):
        weight = lax.all_gather(weight, name, axis=0, tiled=True)
    weight, group_qkv = lax.optimization_barrier((weight, group_qkv))
    weight = lax.all_gather(weight, DP[1], axis=0, tiled=True)

    local_qkv = group_qkv.reshape(tokens_here, fsdp_count, heads_here * 3 * HD)
    gathered_qkv = lax.all_to_all(local_qkv, FSDP, split_axis=1, concat_axis=0, tiled=True)
    group_len = tokens_here * fsdp_count
    gathered_qkv = gathered_qkv.reshape(group_len, heads_here * 3 * HD)

    request_ids = jnp.arange(requests, dtype=jnp.int32)
    member = (page_request[:, None] == request_ids[None, :]).astype(jnp.int32)
    slot_rank = jnp.sum(member * (jnp.cumsum(member, axis=0) - 1), axis=1)
    target_host = jnp.sum(member * request_host[None, :], axis=1)
    is_live = jnp.sum(member, axis=1)
    target_slot = jnp.where(is_live > 0, target_host * MOST + slot_rank, -1)
    chosen = target_slot[:, None] == jnp.arange(requests * MOST, dtype=jnp.int32)[None, :]
    flat_pool = cache_pool.reshape(slot_count, PAGE * features)
    packed = jnp.einsum(
        "sp,sf->pf", chosen.astype(jnp.bfloat16), flat_pool, preferred_element_type=jnp.float32
    )
    occupied = jnp.sum(chosen.astype(jnp.int32), axis=0) > 0
    packed = jnp.where(occupied[:, None], packed, jnp.nan)
    packed = packed.astype(jnp.bfloat16).reshape(requests, MOST, PAGE, features)
    weight, packed, gathered_qkv = lax.optimization_barrier((weight, packed, gathered_qkv))
    weight = lax.all_gather(weight, DP[0], axis=0, tiled=True)
    weight = lax.all_gather(weight, FSDP[0], axis=0, tiled=True)
    arrived = lax.all_to_all(packed, DP, split_axis=0, concat_axis=0, tiled=True)
    present = jnp.logical_not(jnp.isnan(arrived[:, :, 0, 0]))
    live_tokens = jnp.repeat(present.reshape(requests * MOST), PAGE)
    cached = arrived.reshape(requests * MOST * PAGE, features)
    attn_heads = attention(gathered_qkv, cached, live_tokens, heads_here, min(256, group_len))
    tokens_attn = lax.all_to_all(attn_heads, FSDP, split_axis=0, concat_axis=1, tiled=True)
    split = [size for _, size in PHYSICAL_SPLIT["dp"] + PHYSICAL_SPLIT["fsdp"]]
    tokens_attn = tokens_attn.reshape(tokens_here, *split, out_weight.shape[0])
    tokens_attn = jnp.transpose(tokens_attn, (0, 4, 1, 2, 3, 5, 6)).reshape(tokens_here, width)
    summed = jnp.dot(tokens_attn, weight, preferred_element_type=jnp.float32)
    return summed.astype(jnp.bfloat16).reshape(1, tokens_here, width)


def solution(mesh):
    split = [part for axis in mesh.axis_names for part in PHYSICAL_SPLIT[axis]]
    fine = Mesh(mesh.devices.reshape([size for _, size in split]), DP + FSDP)
    return jax.shard_map(
        lambda *args: per_device(
            *args, fsdp_count=mesh.shape["fsdp"], dp_count=mesh.shape["dp"]
        ),
        mesh=fine,
        in_specs=(
            P(DP, FSDP, None),
            P(DP, None, FSDP),
            P(DP),
            P(),
            P(DP + FSDP, None),
        ),
        out_specs=P(DP, FSDP, None),
        check_vma=False,
    )
```

```python
import functools
import math

import jax
import jax.numpy as jnp
from jax import lax
from jax.experimental import pallas as pl
from jax.experimental.pallas import tpu as pltpu
from jax.sharding import Mesh, PartitionSpec as P

HD = 128
PAGE = 16
MOST = 2

PHYSICAL_SPLIT = {"dp": (("x", 4), ("z", 8), ("y_lo", 2)), "fsdp": (("y_hi", 4), ("core", 2))}
DP = tuple(name for name, _ in PHYSICAL_SPLIT["dp"])
FSDP = tuple(name for name, _ in PHYSICAL_SPLIT["fsdp"])


def attention_kernel(q_ref, kc_ref, vc_ref, kn_ref, vn_ref, live_row_ref, live_col_ref, out_ref, *, scale):
    rows = q_ref.shape[0]
    first = pl.program_id(1) * rows
    contract = (((1,), (1,)), ((), ()))
    q = q_ref[...]
    cache_scores = lax.dot_general(q, kc_ref[...], contract, preferred_element_type=jnp.float32) * scale
    cache_scores = jnp.where(live_row_ref[...] > 0, cache_scores, -jnp.inf)
    group_scores = lax.dot_general(q, kn_ref[...], contract, preferred_element_type=jnp.float32) * scale
    row = first + lax.broadcasted_iota(jnp.int32, group_scores.shape, 0)
    col = lax.broadcasted_iota(jnp.int32, group_scores.shape, 1)
    group_scores = jnp.where(col <= row, group_scores, -jnp.inf)
    row_max = jnp.maximum(
        jnp.max(cache_scores, axis=1, keepdims=True), jnp.max(group_scores, axis=1, keepdims=True)
    )
    cache_expo = jnp.exp(cache_scores - row_max)
    group_expo = jnp.exp(group_scores - row_max)
    row_total = jnp.sum(cache_expo, axis=1, keepdims=True) + jnp.sum(group_expo, axis=1, keepdims=True)
    values = jnp.where(live_col_ref[...] > 0, vc_ref[...], jnp.zeros((), vc_ref.dtype))
    mixture = jnp.dot(cache_expo.astype(jnp.bfloat16), values, preferred_element_type=jnp.float32)
    mixture = mixture + jnp.dot(
        group_expo.astype(jnp.bfloat16), vn_ref[...], preferred_element_type=jnp.float32
    )
    out_ref[...] = (mixture / row_total).astype(out_ref.dtype)


def attention(qkv, cache, live, heads, block_rows):
    group = qkv.shape[0]
    keys = cache.shape[0]
    live = live.astype(jnp.float32)
    flops = 4 * heads * group * (keys + group) * HD
    return pl.pallas_call(
        functools.partial(attention_kernel, scale=1.0 / math.sqrt(HD)),
        grid=(heads, group // block_rows),
        in_specs=[
            pl.BlockSpec((block_rows, HD), lambda h, b: (b, 3 * h)),
            pl.BlockSpec((keys, HD), lambda h, b: (0, 2 * h)),
            pl.BlockSpec((keys, HD), lambda h, b: (0, 2 * h + 1)),
            pl.BlockSpec((group, HD), lambda h, b: (0, 3 * h + 1)),
            pl.BlockSpec((group, HD), lambda h, b: (0, 3 * h + 2)),
            pl.BlockSpec((1, keys), lambda h, b: (0, 0)),
            pl.BlockSpec((keys, 1), lambda h, b: (0, 0)),
        ],
        out_specs=pl.BlockSpec((block_rows, HD), lambda h, b: (b, h)),
        out_shape=jax.ShapeDtypeStruct((group, heads * HD), qkv.dtype),
        cost_estimate=pl.CostEstimate(
            flops=flops,
            transcendentals=heads * group * (keys + group),
            bytes_accessed=2 * (qkv.size + cache.size + group * heads * HD),
        ),
    )(qkv, cache, cache, qkv, qkv, live.reshape(1, keys), live.reshape(keys, 1))


def per_device(group_qkv, cache_pool, page_request, request_host, out_weight, *, fsdp_count, dp_count):
    requests = request_host.shape[0]
    slot_count = page_request.shape[0]
    tokens_here = group_qkv.shape[1]
    features = cache_pool.shape[2]
    heads_here = features // (2 * HD)
    score_scale = 1.0 / math.sqrt(HD)
    width = out_weight.shape[1]

    weight = out_weight
    for name in reversed(DP[2:] + FSDP):
        weight = lax.all_gather(weight, name, axis=0, tiled=True)
    weight, group_qkv = lax.optimization_barrier((weight, group_qkv))
    weight = lax.all_gather(weight, DP[0], axis=0, tiled=True)

    local_qkv = group_qkv.reshape(tokens_here, fsdp_count, heads_here * 3 * HD)
    gathered_qkv = lax.all_to_all(local_qkv, FSDP, split_axis=1, concat_axis=0, tiled=True)
    group_len = tokens_here * fsdp_count
    gathered_qkv = gathered_qkv.reshape(group_len, heads_here * 3 * HD)

    request_ids = jnp.arange(requests, dtype=jnp.int32)
    member = (page_request[:, None] == request_ids[None, :]).astype(jnp.int32)
    slot_rank = jnp.sum(member * (jnp.cumsum(member, axis=0) - 1), axis=1)
    target_host = jnp.sum(member * request_host[None, :], axis=1)
    is_live = jnp.sum(member, axis=1)
    target_slot = jnp.where(is_live > 0, target_host * MOST + slot_rank, -1)
    chosen = target_slot[:, None] == jnp.arange(requests * MOST, dtype=jnp.int32)[None, :]
    flat_pool = cache_pool.reshape(slot_count, PAGE * features)
    packed = jnp.einsum(
        "sp,sf->pf", chosen.astype(jnp.bfloat16), flat_pool, preferred_element_type=jnp.float32
    )
    occupied = jnp.sum(chosen.astype(jnp.int32), axis=0) > 0
    packed = jnp.where(occupied[:, None], packed, jnp.nan)
    packed = packed.astype(jnp.bfloat16).reshape(requests, MOST, PAGE, features)
    weight, packed, gathered_qkv = lax.optimization_barrier((weight, packed, gathered_qkv))
    weight = lax.all_gather(weight, DP[1], axis=0, tiled=True)
    arrived = lax.all_to_all(packed, DP, split_axis=0, concat_axis=0, tiled=True)
    present = jnp.logical_not(jnp.isnan(arrived[:, :, 0, 0]))
    live_tokens = jnp.repeat(present.reshape(requests * MOST), PAGE)
    cached = arrived.reshape(requests * MOST * PAGE, features)
    attn_heads = attention(gathered_qkv, cached, live_tokens, heads_here, min(256, group_len))
    tokens_attn = lax.all_to_all(attn_heads, FSDP, split_axis=0, concat_axis=1, tiled=True)
    outer = [size for _, size in PHYSICAL_SPLIT["dp"][:2]]
    tokens_attn = tokens_attn.reshape(tokens_here, *outer, width // math.prod(outer))
    tokens_attn = jnp.transpose(tokens_attn, (0, 2, 1, 3)).reshape(tokens_here, width)
    summed = jnp.dot(tokens_attn, weight, preferred_element_type=jnp.float32)
    return summed.astype(jnp.bfloat16).reshape(1, tokens_here, width)


def solution(mesh):
    split = [part for axis in mesh.axis_names for part in PHYSICAL_SPLIT[axis]]
    fine = Mesh(mesh.devices.reshape([size for _, size in split]), DP + FSDP)
    return jax.shard_map(
        lambda *args: per_device(
            *args, fsdp_count=mesh.shape["fsdp"], dp_count=mesh.shape["dp"]
        ),
        mesh=fine,
        in_specs=(
            P(DP, FSDP, None),
            P(DP, None, FSDP),
            P(DP),
            P(),
            P(DP + FSDP, None),
        ),
        out_specs=P(DP, FSDP, None),
        check_vma=False,
    )
```

```python
import functools
import math

import jax
import jax.numpy as jnp
from jax import lax
from jax.experimental import pallas as pl
from jax.experimental.pallas import tpu as pltpu
from jax.sharding import Mesh, PartitionSpec as P

HD = 128
PAGE = 16
MOST = 2

PHYSICAL_SPLIT = {"dp": (("x", 4), ("z", 8), ("y_lo", 2)), "fsdp": (("y_hi", 4), ("core", 2))}
DP = tuple(name for name, _ in PHYSICAL_SPLIT["dp"])
FSDP = tuple(name for name, _ in PHYSICAL_SPLIT["fsdp"])


def attention_kernel(q_ref, kc_ref, vc_ref, kn_ref, vn_ref, live_row_ref, live_col_ref, out_ref, *, scale):
    rows = q_ref.shape[0]
    first = pl.program_id(1) * rows
    contract = (((1,), (1,)), ((), ()))
    q = q_ref[...]
    cache_scores = lax.dot_general(q, kc_ref[...], contract, preferred_element_type=jnp.float32) * scale
    cache_scores = jnp.where(live_row_ref[...] > 0, cache_scores, -jnp.inf)
    group_scores = lax.dot_general(q, kn_ref[...], contract, preferred_element_type=jnp.float32) * scale
    row = first + lax.broadcasted_iota(jnp.int32, group_scores.shape, 0)
    col = lax.broadcasted_iota(jnp.int32, group_scores.shape, 1)
    group_scores = jnp.where(col <= row, group_scores, -jnp.inf)
    row_max = jnp.maximum(
        jnp.max(cache_scores, axis=1, keepdims=True), jnp.max(group_scores, axis=1, keepdims=True)
    )
    cache_expo = jnp.exp(cache_scores - row_max)
    group_expo = jnp.exp(group_scores - row_max)
    row_total = jnp.sum(cache_expo, axis=1, keepdims=True) + jnp.sum(group_expo, axis=1, keepdims=True)
    values = jnp.where(live_col_ref[...] > 0, vc_ref[...], jnp.zeros((), vc_ref.dtype))
    mixture = jnp.dot(cache_expo.astype(jnp.bfloat16), values, preferred_element_type=jnp.float32)
    mixture = mixture + jnp.dot(
        group_expo.astype(jnp.bfloat16), vn_ref[...], preferred_element_type=jnp.float32
    )
    out_ref[...] = (mixture / row_total).astype(out_ref.dtype)


def attention(qkv, cache, live, heads, block_rows):
    group = qkv.shape[0]
    keys = cache.shape[0]
    live = live.astype(jnp.float32)
    flops = 4 * heads * group * (keys + group) * HD
    return pl.pallas_call(
        functools.partial(attention_kernel, scale=1.0 / math.sqrt(HD)),
        grid=(heads, group // block_rows),
        in_specs=[
            pl.BlockSpec((block_rows, HD), lambda h, b: (b, 3 * h)),
            pl.BlockSpec((keys, HD), lambda h, b: (0, 2 * h)),
            pl.BlockSpec((keys, HD), lambda h, b: (0, 2 * h + 1)),
            pl.BlockSpec((group, HD), lambda h, b: (0, 3 * h + 1)),
            pl.BlockSpec((group, HD), lambda h, b: (0, 3 * h + 2)),
            pl.BlockSpec((1, keys), lambda h, b: (0, 0)),
            pl.BlockSpec((keys, 1), lambda h, b: (0, 0)),
        ],
        out_specs=pl.BlockSpec((block_rows, HD), lambda h, b: (b, h)),
        out_shape=jax.ShapeDtypeStruct((group, heads * HD), qkv.dtype),
        cost_estimate=pl.CostEstimate(
            flops=flops,
            transcendentals=heads * group * (keys + group),
            bytes_accessed=2 * (qkv.size + cache.size + group * heads * HD),
        ),
    )(qkv, cache, cache, qkv, qkv, live.reshape(1, keys), live.reshape(keys, 1))


def per_device(group_qkv, cache_pool, page_request, request_host, out_weight, *, fsdp_count, dp_count):
    requests = request_host.shape[0]
    slot_count = page_request.shape[0]
    tokens_here = group_qkv.shape[1]
    features = cache_pool.shape[2]
    heads_here = features // (2 * HD)
    score_scale = 1.0 / math.sqrt(HD)
    width = out_weight.shape[1]

    weight = out_weight
    for name in reversed(DP[2:] + FSDP):
        weight = lax.all_gather(weight, name, axis=0, tiled=True)
    weight, group_qkv = lax.optimization_barrier((weight, group_qkv))
    weight = lax.all_gather(weight, DP[1], axis=0, tiled=True)

    local_qkv = group_qkv.reshape(tokens_here, fsdp_count, heads_here * 3 * HD)
    gathered_qkv = lax.all_to_all(local_qkv, FSDP, split_axis=1, concat_axis=0, tiled=True)
    group_len = tokens_here * fsdp_count
    gathered_qkv = gathered_qkv.reshape(group_len, heads_here * 3 * HD)

    request_ids = jnp.arange(requests, dtype=jnp.int32)
    member = (page_request[:, None] == request_ids[None, :]).astype(jnp.int32)
    slot_rank = jnp.sum(member * (jnp.cumsum(member, axis=0) - 1), axis=1)
    target_host = jnp.sum(member * request_host[None, :], axis=1)
    is_live = jnp.sum(member, axis=1)
    target_slot = jnp.where(is_live > 0, target_host * MOST + slot_rank, -1)
    chosen = target_slot[:, None] == jnp.arange(requests * MOST, dtype=jnp.int32)[None, :]
    flat_pool = cache_pool.reshape(slot_count, PAGE * features)
    packed = jnp.einsum(
        "sp,sf->pf", chosen.astype(jnp.bfloat16), flat_pool, preferred_element_type=jnp.float32
    )
    occupied = jnp.sum(chosen.astype(jnp.int32), axis=0) > 0
    packed = jnp.where(occupied[:, None], packed, jnp.nan)
    packed = packed.astype(jnp.bfloat16).reshape(requests, MOST, PAGE, features)
    weight, packed, gathered_qkv = lax.optimization_barrier((weight, packed, gathered_qkv))
    half = weight.shape[0] // 2
    weight = lax.dynamic_slice_in_dim(weight, lax.axis_index(FSDP[-1]) * half, half, axis=0)
    weight = lax.all_gather(weight, DP[0], axis=0, tiled=True)
    arrived = lax.all_to_all(packed, DP, split_axis=0, concat_axis=0, tiled=True)
    weight, arrived = lax.optimization_barrier((weight, arrived))
    weight = lax.all_gather(weight, FSDP[-1], axis=0, tiled=True)
    present = jnp.logical_not(jnp.isnan(arrived[:, :, 0, 0]))
    live_tokens = jnp.repeat(present.reshape(requests * MOST), PAGE)
    cached = arrived.reshape(requests * MOST * PAGE, features)
    attn_heads = attention(gathered_qkv, cached, live_tokens, heads_here, min(256, group_len))
    tokens_attn = lax.all_to_all(attn_heads, FSDP, split_axis=0, concat_axis=1, tiled=True)
    tokens_attn = tokens_attn.reshape(tokens_here, lax.axis_size(DP[0]), 2, half)
    tokens_attn = jnp.transpose(tokens_attn, (0, 2, 1, 3)).reshape(tokens_here, width)
    summed = jnp.dot(tokens_attn, weight, preferred_element_type=jnp.float32)
    return summed.astype(jnp.bfloat16).reshape(1, tokens_here, width)


def solution(mesh):
    split = [part for axis in mesh.axis_names for part in PHYSICAL_SPLIT[axis]]
    fine = Mesh(mesh.devices.reshape([size for _, size in split]), DP + FSDP)
    return jax.shard_map(
        lambda *args: per_device(
            *args, fsdp_count=mesh.shape["fsdp"], dp_count=mesh.shape["dp"]
        ),
        mesh=fine,
        in_specs=(
            P(DP, FSDP, None),
            P(DP, None, FSDP),
            P(DP),
            P(),
            P(DP + FSDP, None),
        ),
        out_specs=P(DP, FSDP, None),
        check_vma=False,
    )
```

```python
import functools
import math

import jax
import jax.numpy as jnp
from jax import lax
from jax.experimental import pallas as pl
from jax.experimental.pallas import tpu as pltpu
from jax.sharding import Mesh, PartitionSpec as P

HD = 128
PAGE = 16
MOST = 2

PHYSICAL_SPLIT = {"dp": (("x", 4), ("z", 8), ("y_lo", 2)), "fsdp": (("y_hi", 4), ("core", 2))}
DP = tuple(name for name, _ in PHYSICAL_SPLIT["dp"])
FSDP = tuple(name for name, _ in PHYSICAL_SPLIT["fsdp"])


def attention_kernel(q_ref, kc_ref, vc_ref, kn_ref, vn_ref, live_row_ref, live_col_ref, out_ref, *, scale):
    rows = q_ref.shape[0]
    first = pl.program_id(1) * rows
    contract = (((1,), (1,)), ((), ()))
    q = q_ref[...]
    cache_scores = lax.dot_general(q, kc_ref[...], contract, preferred_element_type=jnp.float32) * scale
    cache_scores = jnp.where(live_row_ref[...] > 0, cache_scores, -jnp.inf)
    group_scores = lax.dot_general(q, kn_ref[...], contract, preferred_element_type=jnp.float32) * scale
    row = first + lax.broadcasted_iota(jnp.int32, group_scores.shape, 0)
    col = lax.broadcasted_iota(jnp.int32, group_scores.shape, 1)
    group_scores = jnp.where(col <= row, group_scores, -jnp.inf)
    row_max = jnp.maximum(
        jnp.max(cache_scores, axis=1, keepdims=True), jnp.max(group_scores, axis=1, keepdims=True)
    )
    cache_expo = jnp.exp(cache_scores - row_max)
    group_expo = jnp.exp(group_scores - row_max)
    row_total = jnp.sum(cache_expo, axis=1, keepdims=True) + jnp.sum(group_expo, axis=1, keepdims=True)
    values = jnp.where(live_col_ref[...] > 0, vc_ref[...], jnp.zeros((), vc_ref.dtype))
    mixture = jnp.dot(cache_expo.astype(jnp.bfloat16), values, preferred_element_type=jnp.float32)
    mixture = mixture + jnp.dot(
        group_expo.astype(jnp.bfloat16), vn_ref[...], preferred_element_type=jnp.float32
    )
    out_ref[...] = (mixture / row_total).astype(out_ref.dtype)


def attention(qkv, cache, live, heads, block_rows):
    group = qkv.shape[0]
    keys = cache.shape[0]
    live = live.astype(jnp.float32)
    flops = 4 * heads * group * (keys + group) * HD
    return pl.pallas_call(
        functools.partial(attention_kernel, scale=1.0 / math.sqrt(HD)),
        grid=(heads, group // block_rows),
        in_specs=[
            pl.BlockSpec((block_rows, HD), lambda h, b: (b, 3 * h)),
            pl.BlockSpec((keys, HD), lambda h, b: (0, 2 * h)),
            pl.BlockSpec((keys, HD), lambda h, b: (0, 2 * h + 1)),
            pl.BlockSpec((group, HD), lambda h, b: (0, 3 * h + 1)),
            pl.BlockSpec((group, HD), lambda h, b: (0, 3 * h + 2)),
            pl.BlockSpec((1, keys), lambda h, b: (0, 0)),
            pl.BlockSpec((keys, 1), lambda h, b: (0, 0)),
        ],
        out_specs=pl.BlockSpec((block_rows, HD), lambda h, b: (b, h)),
        out_shape=jax.ShapeDtypeStruct((group, heads * HD), qkv.dtype),
        cost_estimate=pl.CostEstimate(
            flops=flops,
            transcendentals=heads * group * (keys + group),
            bytes_accessed=2 * (qkv.size + cache.size + group * heads * HD),
        ),
    )(qkv, cache, cache, qkv, qkv, live.reshape(1, keys), live.reshape(keys, 1))


def ring_gather(block, name):
    n = lax.axis_size(name)
    assert n == 4
    forward = [(i, (i + 1) % n) for i in range(n)]
    backward = [(i, (i - 1) % n) for i in range(n)]
    from_prev = lax.ppermute(block, name, forward)
    from_next = lax.ppermute(block, name, backward)
    from_opposite = lax.ppermute(from_prev, name, forward)
    stack = jnp.stack([block, from_next, from_opposite, from_prev])
    stack = jnp.roll(stack, lax.axis_index(name), axis=0)
    return stack.reshape(n * block.shape[0], *block.shape[1:])


def per_device(group_qkv, cache_pool, page_request, request_host, out_weight, *, fsdp_count, dp_count):
    requests = request_host.shape[0]
    slot_count = page_request.shape[0]
    tokens_here = group_qkv.shape[1]
    features = cache_pool.shape[2]
    heads_here = features // (2 * HD)
    score_scale = 1.0 / math.sqrt(HD)
    width = out_weight.shape[1]

    weight = lax.all_gather(out_weight, FSDP[1], axis=0, tiled=True)
    weight = ring_gather(weight, FSDP[0])
    weight = lax.all_gather(weight, DP[2], axis=0, tiled=True)
    weight, group_qkv = lax.optimization_barrier((weight, group_qkv))
    weight = lax.all_gather(weight, DP[1], axis=0, tiled=True)

    local_qkv = group_qkv.reshape(tokens_here, fsdp_count, heads_here * 3 * HD)
    gathered_qkv = lax.all_to_all(local_qkv, FSDP, split_axis=1, concat_axis=0, tiled=True)
    group_len = tokens_here * fsdp_count
    gathered_qkv = gathered_qkv.reshape(group_len, heads_here * 3 * HD)

    request_ids = jnp.arange(requests, dtype=jnp.int32)
    member = (page_request[:, None] == request_ids[None, :]).astype(jnp.int32)
    slot_rank = jnp.sum(member * (jnp.cumsum(member, axis=0) - 1), axis=1)
    target_host = jnp.sum(member * request_host[None, :], axis=1)
    is_live = jnp.sum(member, axis=1)
    target_slot = jnp.where(is_live > 0, target_host * MOST + slot_rank, -1)
    chosen = target_slot[:, None] == jnp.arange(requests * MOST, dtype=jnp.int32)[None, :]
    flat_pool = cache_pool.reshape(slot_count, PAGE * features)
    packed = jnp.einsum(
        "sp,sf->pf", chosen.astype(jnp.bfloat16), flat_pool, preferred_element_type=jnp.float32
    )
    occupied = jnp.sum(chosen.astype(jnp.int32), axis=0) > 0
    packed = jnp.where(occupied[:, None], packed, jnp.nan)
    packed = packed.astype(jnp.bfloat16).reshape(requests, MOST, PAGE, features)
    weight, packed, gathered_qkv = lax.optimization_barrier((weight, packed, gathered_qkv))
    weight = lax.all_gather(weight, DP[0], axis=0, tiled=True)
    arrived = lax.all_to_all(packed, DP, split_axis=0, concat_axis=0, tiled=True)
    present = jnp.logical_not(jnp.isnan(arrived[:, :, 0, 0]))
    live_tokens = jnp.repeat(present.reshape(requests * MOST), PAGE)
    cached = arrived.reshape(requests * MOST * PAGE, features)
    attn_heads = attention(gathered_qkv, cached, live_tokens, heads_here, min(256, group_len))
    tokens_attn = lax.all_to_all(attn_heads, FSDP, split_axis=0, concat_axis=1, tiled=True)
    summed = jnp.dot(tokens_attn, weight, preferred_element_type=jnp.float32)
    return summed.astype(jnp.bfloat16).reshape(1, tokens_here, width)


def solution(mesh):
    split = [part for axis in mesh.axis_names for part in PHYSICAL_SPLIT[axis]]
    fine = Mesh(mesh.devices.reshape([size for _, size in split]), DP + FSDP)
    return jax.shard_map(
        lambda *args: per_device(
            *args, fsdp_count=mesh.shape["fsdp"], dp_count=mesh.shape["dp"]
        ),
        mesh=fine,
        in_specs=(
            P(DP, FSDP, None),
            P(DP, None, FSDP),
            P(DP),
            P(),
            P(DP + FSDP, None),
        ),
        out_specs=P(DP, FSDP, None),
        check_vma=False,
    )
```

```python
import functools
import math

import jax
import jax.numpy as jnp
from jax import lax
from jax.experimental import pallas as pl
from jax.experimental.pallas import tpu as pltpu
from jax.sharding import Mesh, PartitionSpec as P

HD = 128
PAGE = 16
MOST = 2

PHYSICAL_SPLIT = {"dp": (("x", 4), ("z", 8), ("y_lo", 2)), "fsdp": (("y_hi", 4), ("core", 2))}
DP = tuple(name for name, _ in PHYSICAL_SPLIT["dp"])
FSDP = tuple(name for name, _ in PHYSICAL_SPLIT["fsdp"])


def attention_kernel(q_ref, kc_ref, vc_ref, kn_ref, vn_ref, live_row_ref, live_col_ref, out_ref, *, scale):
    rows = q_ref.shape[0]
    first = pl.program_id(1) * rows
    contract = (((1,), (1,)), ((), ()))
    q = q_ref[...]
    cache_scores = lax.dot_general(q, kc_ref[...], contract, preferred_element_type=jnp.float32) * scale
    cache_scores = jnp.where(live_row_ref[...] > 0, cache_scores, -jnp.inf)
    group_scores = lax.dot_general(q, kn_ref[...], contract, preferred_element_type=jnp.float32) * scale
    row = first + lax.broadcasted_iota(jnp.int32, group_scores.shape, 0)
    col = lax.broadcasted_iota(jnp.int32, group_scores.shape, 1)
    group_scores = jnp.where(col <= row, group_scores, -jnp.inf)
    row_max = jnp.maximum(
        jnp.max(cache_scores, axis=1, keepdims=True), jnp.max(group_scores, axis=1, keepdims=True)
    )
    cache_expo = jnp.exp(cache_scores - row_max)
    group_expo = jnp.exp(group_scores - row_max)
    row_total = jnp.sum(cache_expo, axis=1, keepdims=True) + jnp.sum(group_expo, axis=1, keepdims=True)
    values = jnp.where(live_col_ref[...] > 0, vc_ref[...], jnp.zeros((), vc_ref.dtype))
    mixture = jnp.dot(cache_expo.astype(jnp.bfloat16), values, preferred_element_type=jnp.float32)
    mixture = mixture + jnp.dot(
        group_expo.astype(jnp.bfloat16), vn_ref[...], preferred_element_type=jnp.float32
    )
    out_ref[...] = (mixture / row_total).astype(out_ref.dtype)


def attention(qkv, cache, live, heads, block_rows):
    group = qkv.shape[0]
    keys = cache.shape[0]
    live = live.astype(jnp.float32)
    flops = 4 * heads * group * (keys + group) * HD
    return pl.pallas_call(
        functools.partial(attention_kernel, scale=1.0 / math.sqrt(HD)),
        grid=(heads, group // block_rows),
        in_specs=[
            pl.BlockSpec((block_rows, HD), lambda h, b: (b, 3 * h)),
            pl.BlockSpec((keys, HD), lambda h, b: (0, 2 * h)),
            pl.BlockSpec((keys, HD), lambda h, b: (0, 2 * h + 1)),
            pl.BlockSpec((group, HD), lambda h, b: (0, 3 * h + 1)),
            pl.BlockSpec((group, HD), lambda h, b: (0, 3 * h + 2)),
            pl.BlockSpec((1, keys), lambda h, b: (0, 0)),
            pl.BlockSpec((keys, 1), lambda h, b: (0, 0)),
        ],
        out_specs=pl.BlockSpec((block_rows, HD), lambda h, b: (b, h)),
        out_shape=jax.ShapeDtypeStruct((group, heads * HD), qkv.dtype),
        cost_estimate=pl.CostEstimate(
            flops=flops,
            transcendentals=heads * group * (keys + group),
            bytes_accessed=2 * (qkv.size + cache.size + group * heads * HD),
        ),
    )(qkv, cache, cache, qkv, qkv, live.reshape(1, keys), live.reshape(keys, 1))


def per_device(group_qkv, cache_pool, page_request, request_host, out_weight, *, fsdp_count, dp_count):
    requests = request_host.shape[0]
    slot_count = page_request.shape[0]
    tokens_here = group_qkv.shape[1]
    features = cache_pool.shape[2]
    heads_here = features // (2 * HD)
    score_scale = 1.0 / math.sqrt(HD)
    width = out_weight.shape[1]

    weight = lax.all_gather(out_weight, DP[2:] + FSDP, axis=0, tiled=True)
    weight, group_qkv = lax.optimization_barrier((weight, group_qkv))
    weight = lax.all_gather(weight, DP[1], axis=0, tiled=True)

    local_qkv = group_qkv.reshape(tokens_here, fsdp_count, heads_here * 3 * HD)
    gathered_qkv = lax.all_to_all(local_qkv, FSDP, split_axis=1, concat_axis=0, tiled=True)
    group_len = tokens_here * fsdp_count
    gathered_qkv = gathered_qkv.reshape(group_len, heads_here * 3 * HD)

    request_ids = jnp.arange(requests, dtype=jnp.int32)
    member = (page_request[:, None] == request_ids[None, :]).astype(jnp.int32)
    slot_rank = jnp.sum(member * (jnp.cumsum(member, axis=0) - 1), axis=1)
    target_host = jnp.sum(member * request_host[None, :], axis=1)
    is_live = jnp.sum(member, axis=1)
    target_slot = jnp.where(is_live > 0, target_host * MOST + slot_rank, -1)
    chosen = target_slot[:, None] == jnp.arange(requests * MOST, dtype=jnp.int32)[None, :]
    flat_pool = cache_pool.reshape(slot_count, PAGE * features)
    packed = jnp.einsum(
        "sp,sf->pf", chosen.astype(jnp.bfloat16), flat_pool, preferred_element_type=jnp.float32
    )
    occupied = jnp.sum(chosen.astype(jnp.int32), axis=0) > 0
    packed = jnp.where(occupied[:, None], packed, jnp.nan)
    packed = packed.astype(jnp.bfloat16).reshape(requests, MOST, PAGE, features)
    weight, packed, gathered_qkv = lax.optimization_barrier((weight, packed, gathered_qkv))
    weight = lax.all_gather(weight, DP[0], axis=0, tiled=True)
    arrived = lax.all_to_all(packed, DP, split_axis=0, concat_axis=0, tiled=True)
    present = jnp.logical_not(jnp.isnan(arrived[:, :, 0, 0]))
    live_tokens = jnp.repeat(present.reshape(requests * MOST), PAGE)
    cached = arrived.reshape(requests * MOST * PAGE, features)
    attn_heads = attention(gathered_qkv, cached, live_tokens, heads_here, min(256, group_len))
    tokens_attn = lax.all_to_all(attn_heads, FSDP, split_axis=0, concat_axis=1, tiled=True)
    summed = jnp.dot(tokens_attn, weight, preferred_element_type=jnp.float32)
    return summed.astype(jnp.bfloat16).reshape(1, tokens_here, width)


def solution(mesh):
    split = [part for axis in mesh.axis_names for part in PHYSICAL_SPLIT[axis]]
    fine = Mesh(mesh.devices.reshape([size for _, size in split]), DP + FSDP)
    return jax.shard_map(
        lambda *args: per_device(
            *args, fsdp_count=mesh.shape["fsdp"], dp_count=mesh.shape["dp"]
        ),
        mesh=fine,
        in_specs=(
            P(DP, FSDP, None),
            P(DP, None, FSDP),
            P(DP),
            P(),
            P(DP + FSDP, None),
        ),
        out_specs=P(DP, FSDP, None),
        check_vma=False,
    )
```
